128 devices in a mesh: chan: 32 (over z, y_lo, x), freq: 4 (over y_hi, core).
Axes of the slice: x: 4, y: 4 (y_hi: 2, y_lo: 2; y = y_hi * 2 + y_lo), z: 4, core: 2. Of those that a mesh axis runs over, the one named last changes fastest.
Arguments:
- strain: bfloat16 [2048, 256, 1024], P('chan', 'freq'), may hold values from -6 to 6
- mad_index: int32 [2048], P('chan'), may hold values from 0 to 15
- mad_table: float32 [16], replicated, may hold values from 0.25 to 2.5
- freq_bins: int32 [64], replicated, may hold values from 1 to 511
- valid_count: int32 [2048], P('chan'), may hold values from 64 to 256
Outputs:
- cross: float32 [64, 2, 2048, 2048], P('freq', None, 'chan')
The draws below stay inside these ranges and needn't reach their ends.
All inputs are finite; a program needn't handle non-finite values.
Results may differ from the reference program's by a relative error of at most 0.0057.
Values may be sent and summed in bfloat16 or wider, within the bound.
No kernel may reach another device: no remote copies, remote signals or barrier semaphores. Data moves between devices by JAX's collectives and lax.ppermute only.
A program may use at most 256 MiB of HBM per device.

```python
import math
import jax
import jax.numpy as jnp
from jax import lax

L = 1024
NF = 64
NT = 16
CHANNELS = 2048
WINDOWS = 256


def with_ends(drawn, rng, least, top_value):
    place = [jax.random.randint(jax.random.fold_in(rng, axis), (), 0, length) for axis, length in enumerate(drawn.shape)]
    widest = drawn.shape.index(max(drawn.shape))
    beside = place[:widest] + [(place[widest] + 1) % drawn.shape[widest]] + place[widest + 1:]
    return drawn.at[tuple(place)].set(least).at[tuple(beside)].set(top_value)


def steps_of(rng, shape, pieces, low, top_value):
    def one(axis_at, shards_of):
        draws = jax.random.uniform(jax.random.fold_in(jax.random.fold_in(rng, 6), axis_at), (shards_of,), jnp.float32, low / len(pieces), top_value / len(pieces))
        return jnp.repeat(jnp.exp(draws), shape[axis_at] // shards_of).reshape((-1,) + (1,) * (len(shape) - axis_at - 1))

    factor_of = one(*pieces[0])
    for cut in pieces[1:]:
        factor_of = factor_of * one(*cut)
    return factor_of


def noise(rng, extent, deviation, limit, pieces=(), kind=jnp.bfloat16):
    loudness = steps_of(rng, extent, pieces, -0.22, 0.18) if pieces else 1.0
    result = jax.random.normal(rng, extent, jnp.float32) * deviation * loudness
    return jnp.minimum(jnp.maximum(result, -limit), limit).astype(kind)


def setup_inputs(seed: int = 0) -> dict:
    key_of = jax.random.split(jax.random.key(seed), 6)
    return {
        "strain": noise(key_of[0], (CHANNELS, WINDOWS, L), 1.0, 6.0, ((0, 32), (1, 4))),
        "mad_index": with_ends(jax.random.randint(key_of[1], (CHANNELS,), 0, NT), jax.random.fold_in(key_of[1], 1), 0, NT - 1).astype(jnp.int32),
        "mad_table": jnp.clip(jnp.exp(jax.random.uniform(key_of[2], (NT,), jnp.float32, math.log(0.25), math.log(2.5))), 0.25, 2.5),
        "freq_bins": with_ends(jax.random.randint(key_of[3], (NF,), 1, L // 2), jax.random.fold_in(key_of[3], 1), 1, (L // 2) - 1).astype(jnp.int32),
        "valid_count": with_ends(jax.random.randint(key_of[4], (CHANNELS,), WINDOWS // 4, WINDOWS + 1), jax.random.fold_in(key_of[4], 1), WINDOWS // 4, WINDOWS).astype(jnp.int32),
    }


CLIP_FACTOR = 2.0

def dft_table(freq_bins, length):
    samples = jnp.arange(length, dtype=jnp.int32)
    phase_index = samples[:, None] * freq_bins[None, :] % length
    angle = phase_index.astype(jnp.float32) * (2.0 * math.pi / length)
    taper = 0.5 - 0.5 * jnp.cos(samples.astype(jnp.float32) * (2.0 * math.pi / length))
    cosine = taper[:, None] * jnp.cos(angle)
    sine = -taper[:, None] * jnp.sin(angle)
    stacked = jnp.stack([cosine, sine], axis=2)
    return stacked.reshape(length, 2 * freq_bins.shape[0]).astype(jnp.bfloat16)

def reference(strain, mad_index, mad_table, freq_bins, valid_count):
    channels, windows, length = strain.shape
    bin_count = freq_bins.shape[0]
    limits = mad_table[mad_index] * CLIP_FACTOR
    table = dft_table(freq_bins, length)

    def per_channel(inputs):
        rows_in, limit_one = inputs
        clipped = jnp.clip(rows_in.astype(jnp.float32), -limit_one, limit_one).astype(jnp.bfloat16)
        return jnp.dot(clipped, table, preferred_element_type=jnp.float32)
    spectrum = lax.map(per_channel, (strain, limits))
    window_ids = jnp.arange(windows, dtype=jnp.int32)
    counts = valid_count.astype(jnp.float32)
    weights = jnp.where(window_ids[None, :] < valid_count[:, None], 1.0 / jnp.sqrt(counts)[:, None], 0.0)
    weighted = (spectrum * weights[:, :, None]).astype(jnp.bfloat16)
    weighted = jnp.transpose(weighted.reshape(channels, windows, bin_count, 2), (2, 3, 0, 1))

    def per_bin(bin_panel):
        stacked = bin_panel.reshape(2 * channels, windows)
        products = jnp.dot(stacked, stacked.T, preferred_element_type=jnp.float32)
        real_part = products[:channels, :channels] + products[channels:, channels:]
        imag_part = products[channels:, :channels] - products[:channels, channels:]
        return jnp.stack([real_part, imag_part])
    return lax.map(per_bin, weighted)
```

```python
import math

import jax
import jax.numpy as jnp
from jax import lax
from jax.sharding import PartitionSpec as P

CLIP_FACTOR = 2.0


def dft_table(freq_bins, length):
    samples = jnp.arange(length, dtype=jnp.int32)
    phase_index = samples[:, None] * freq_bins[None, :] % length
    angle = phase_index.astype(jnp.float32) * (2.0 * math.pi / length)
    taper = 0.5 - 0.5 * jnp.cos(samples.astype(jnp.float32) * (2.0 * math.pi / length))
    cosine = taper[:, None] * jnp.cos(angle)
    sine = -taper[:, None] * jnp.sin(angle)
    stacked = jnp.stack([cosine, sine], axis=2)
    return stacked.reshape(length, 2 * freq_bins.shape[0]).astype(jnp.bfloat16)


def clip_scales(mad_index, mad_table):
    entries = jnp.arange(mad_table.shape[0], dtype=jnp.int32)
    matches = mad_index[:, None] == entries[None, :]
    return jnp.sum(jnp.where(matches, mad_table[None, :], 0.0), axis=1)


def row_operand(panel):
    first, second = panel[:, 0], panel[:, 1]
    real_rows = jnp.stack([first, second], axis=2)
    imag_rows = jnp.stack([second, -first], axis=2)
    return jnp.stack([real_rows, imag_rows], axis=1)


def per_device(strain, mad_index, mad_table, freq_bins, valid_count):
    channels, win_local, length = strain.shape
    bin_count = freq_bins.shape[0]
    limits = (clip_scales(mad_index, mad_table) * CLIP_FACTOR)[:, None, None]
    clipped = jnp.clip(strain.astype(jnp.float32), -limits, limits).astype(jnp.bfloat16)
    table = dft_table(freq_bins, length)
    flat_rows = clipped.reshape(channels * win_local, length)
    spectrum = lax.dot_general(
        table, flat_rows, (((0,), (1,)), ((), ())), preferred_element_type=jnp.float32
    )
    window_ids = lax.axis_index("freq") * win_local + jnp.arange(win_local, dtype=jnp.int32)
    counts = valid_count.astype(jnp.float32)
    weights = jnp.where(
        window_ids[None, :] < valid_count[:, None], 1.0 / jnp.sqrt(counts)[:, None], 0.0
    )
    weighted = (spectrum * weights.reshape(1, channels * win_local)).astype(jnp.bfloat16)
    weighted = weighted.reshape(bin_count, 2, channels, win_local)
    panels = lax.all_to_all(weighted, "freq", split_axis=0, concat_axis=3, tiled=True)
    columns = lax.all_gather(panels, "chan", axis=2, tiled=True)
    rows = row_operand(panels)
    return jnp.einsum(
        "fqipw,fpjw->fqij", rows, columns, preferred_element_type=jnp.float32
    )


def solution(mesh):
    return jax.shard_map(
        per_device,
        mesh=mesh,
        in_specs=(P("chan", "freq", None), P("chan"), P(), P(), P("chan")),
        out_specs=P("freq", None, "chan", None),
        check_vma=False,
    )
```

```python
import math

import jax
import jax.numpy as jnp
from jax import lax
from jax.sharding import Mesh, PartitionSpec as P

CLIP_FACTOR = 2.0


def dft_table(freq_bins, length):
    samples = jnp.arange(length, dtype=jnp.int32)
    phase_index = samples[:, None] * freq_bins[None, :] % length
    angle = phase_index.astype(jnp.float32) * (2.0 * math.pi / length)
    taper = 0.5 - 0.5 * jnp.cos(samples.astype(jnp.float32) * (2.0 * math.pi / length))
    cosine = taper[:, None] * jnp.cos(angle)
    sine = -taper[:, None] * jnp.sin(angle)
    stacked = jnp.stack([cosine, sine], axis=2)
    return stacked.reshape(length, 2 * freq_bins.shape[0]).astype(jnp.bfloat16)


def clip_scales(mad_index, mad_table):
    entries = jnp.arange(mad_table.shape[0], dtype=jnp.int32)
    matches = mad_index[:, None] == entries[None, :]
    return jnp.sum(jnp.where(matches, mad_table[None, :], 0.0), axis=1)


def row_operand(panel):
    first, second = panel[:, 0], panel[:, 1]
    real_rows = jnp.stack([first, second], axis=2)
    imag_rows = jnp.stack([second, -first], axis=2)
    return jnp.stack([real_rows, imag_rows], axis=1)


def shifted(block, axis, distance):
    size = lax.axis_size(axis)
    return lax.ppermute(block, axis, [((i + distance) % size, i) for i in range(size)])


def ring_gather(block, axis, split_axis):
    ahead = shifted(block, axis, 1)
    behind = shifted(block, axis, -1)
    half = block.shape[split_axis] // 2
    far_a = shifted(lax.slice_in_dim(ahead, 0, half, axis=split_axis), axis, 1)
    far_b = shifted(lax.slice_in_dim(behind, half, 2 * half, axis=split_axis), axis, -1)
    far = jnp.concatenate([far_a, far_b], axis=split_axis)
    return [block, ahead, far, behind]


def per_device(strain, mad_index, mad_table, freq_bins, valid_count):
    channels, win_local, length = strain.shape
    bin_count = freq_bins.shape[0]
    limits = (clip_scales(mad_index, mad_table) * CLIP_FACTOR)[:, None, None]
    clipped = jnp.clip(strain.astype(jnp.float32), -limits, limits).astype(jnp.bfloat16)
    table = dft_table(freq_bins, length)
    flat_rows = clipped.reshape(channels * win_local, length)
    spectrum = lax.dot_general(
        table, flat_rows, (((0,), (1,)), ((), ())), preferred_element_type=jnp.float32
    )
    freq_index = lax.axis_index("yhi") * lax.axis_size("core") + lax.axis_index("core")
    window_ids = freq_index * win_local + jnp.arange(win_local, dtype=jnp.int32)
    counts = valid_count.astype(jnp.float32)
    weights = jnp.where(
        window_ids[None, :] < valid_count[:, None], 1.0 / jnp.sqrt(counts)[:, None], 0.0
    )
    weighted = (spectrum * weights.reshape(1, channels * win_local)).astype(jnp.bfloat16)
    groups = lax.axis_size("yhi") * lax.axis_size("core")
    pairs = lax.axis_size("ylo")
    bins_local = bin_count // groups
    weighted = weighted.reshape(groups, bins_local, 2, channels, win_local)
    outgoing = jnp.broadcast_to(weighted[None], (pairs,) + weighted.shape)
    outgoing = outgoing.reshape((pairs * groups,) + weighted.shape[1:])
    incoming = lax.all_to_all(outgoing, ("ylo", "yhi", "core"), 0, 0, tiled=True)
    incoming = incoming.reshape(pairs, groups, bins_local, 2, channels, win_local)
    panel = jnp.transpose(incoming, (2, 3, 0, 4, 1, 5)).reshape(
        bins_local, 2, pairs * channels, groups * win_local
    )
    own = lax.dynamic_slice_in_dim(panel, lax.axis_index("ylo") * channels, channels, axis=2)
    rows = row_operand(own)

    split = bins_local // 2
    first = [jnp.stack(ring_gather(p, "x", 3)) for p in [panel[:split]]][0]
    second = [jnp.stack(ring_gather(p, "z", 3)) for p in [panel[split:]]][0]
    first = jnp.stack(ring_gather(first, "z", 4))
    second = jnp.stack(ring_gather(second, "x", 4))
    second = jnp.swapaxes(second, 0, 1)
    gathered = jnp.concatenate([first, second], axis=2)
    zs, xs = gathered.shape[0], gathered.shape[1]
    gathered = gathered.reshape(zs, xs, bins_local, 2, pairs, channels, groups * win_local)
    products = jnp.einsum(
        "fqipw,ZXfpYcw->fqiZYXc", rows, gathered, preferred_element_type=jnp.float32
    )
    z_shift = (zs - lax.axis_index("z")) % zs
    x_shift = (xs - lax.axis_index("x")) % xs
    products = jnp.concatenate([products, products], axis=3)
    products = lax.dynamic_slice_in_dim(products, z_shift, zs, axis=3)
    products = jnp.concatenate([products, products], axis=5)
    products = lax.dynamic_slice_in_dim(products, x_shift, xs, axis=5)
    return products.reshape(bins_local, 2, channels, zs * pairs * xs * channels)


def solution(mesh):
    sizes = dict(zip(mesh.axis_names, mesh.devices.shape))
    chan, freq = sizes["chan"], sizes["freq"]
    devices = mesh.devices.reshape(chan // 8, 2, 4, freq // 2, 2)
    grid = Mesh(devices, ("z", "ylo", "x", "yhi", "core"))
    chan_axes = ("z", "ylo", "x")
    freq_axes = ("yhi", "core")
    return jax.shard_map(
        per_device,
        mesh=grid,
        in_specs=(P(chan_axes, freq_axes, None), P(chan_axes), P(), P(), P(chan_axes)),
        out_specs=P(freq_axes, None, chan_axes, None),
        check_vma=False,
    )
```

```python
import math

import jax
import jax.numpy as jnp
from jax import lax
from jax.sharding import Mesh, PartitionSpec as P

CLIP_FACTOR = 2.0


def dft_table(freq_bins, length):
    samples = jnp.arange(length, dtype=jnp.int32)
    phase_index = samples[:, None] * freq_bins[None, :] % length
    angle = phase_index.astype(jnp.float32) * (2.0 * math.pi / length)
    taper = 0.5 - 0.5 * jnp.cos(samples.astype(jnp.float32) * (2.0 * math.pi / length))
    cosine = taper[:, None] * jnp.cos(angle)
    sine = -taper[:, None] * jnp.sin(angle)
    stacked = jnp.stack([cosine, sine], axis=2)
    return stacked.reshape(length, 2 * freq_bins.shape[0]).astype(jnp.bfloat16)


def clip_scales(mad_index, mad_table):
    entries = jnp.arange(mad_table.shape[0], dtype=jnp.int32)
    matches = mad_index[:, None] == entries[None, :]
    return jnp.sum(jnp.where(matches, mad_table[None, :], 0.0), axis=1)


def row_operand(panel):
    first, second = panel[:, 0], panel[:, 1]
    real_rows = jnp.stack([first, second], axis=2)
    imag_rows = jnp.stack([second, -first], axis=2)
    return jnp.stack([real_rows, imag_rows], axis=1)


def shifted(block, axis, distance):
    size = lax.axis_size(axis)
    return lax.ppermute(block, axis, [((i + distance) % size, i) for i in range(size)])


def ring_gather(block, axis, split_axis):
    ahead = shifted(block, axis, 1)
    behind = shifted(block, axis, -1)
    half = block.shape[split_axis] // 2
    far_a = shifted(lax.slice_in_dim(ahead, 0, half, axis=split_axis), axis, 1)
    far_b = shifted(lax.slice_in_dim(behind, half, 2 * half, axis=split_axis), axis, -1)
    far = jnp.concatenate([far_a, far_b], axis=split_axis)
    return [block, ahead, far, behind]


def ordered_by_position(slots, axis, stack_axis):
    size = len(slots)

    def arrangement(at):
        return lambda *blocks: jnp.stack(
            [blocks[(k - at) % size] for k in range(size)], axis=stack_axis
        )

    return lax.switch(lax.axis_index(axis), [arrangement(at) for at in range(size)], *slots)


def per_device(strain, mad_index, mad_table, freq_bins, valid_count):
    channels, win_local, length = strain.shape
    bin_count = freq_bins.shape[0]
    limits = (clip_scales(mad_index, mad_table) * CLIP_FACTOR)[:, None, None]
    clipped = jnp.clip(strain.astype(jnp.float32), -limits, limits).astype(jnp.bfloat16)
    table = dft_table(freq_bins, length)
    flat_rows = clipped.reshape(channels * win_local, length)
    spectrum = lax.dot_general(
        table, flat_rows, (((0,), (1,)), ((), ())), preferred_element_type=jnp.float32
    )
    freq_index = lax.axis_index("yhi") * lax.axis_size("core") + lax.axis_index("core")
    window_ids = freq_index * win_local + jnp.arange(win_local, dtype=jnp.int32)
    counts = valid_count.astype(jnp.float32)
    weights = jnp.where(
        window_ids[None, :] < valid_count[:, None], 1.0 / jnp.sqrt(counts)[:, None], 0.0
    )
    weighted = (spectrum * weights.reshape(1, channels * win_local)).astype(jnp.bfloat16)
    groups = lax.axis_size("yhi") * lax.axis_size("core")
    pairs = lax.axis_size("ylo")
    bins_local = bin_count // groups
    weighted = weighted.reshape(groups, bins_local, 2, channels, win_local)
    outgoing = jnp.broadcast_to(weighted[None], (pairs,) + weighted.shape)
    outgoing = outgoing.reshape((pairs * groups,) + weighted.shape[1:])
    incoming = lax.all_to_all(outgoing, ("ylo", "yhi", "core"), 0, 0, tiled=True)
    incoming = incoming.reshape(pairs, groups, bins_local, 2, channels, win_local)
    panel = jnp.transpose(incoming, (2, 3, 0, 4, 1, 5)).reshape(
        bins_local, 2, pairs * channels, groups * win_local
    )
    own = lax.dynamic_slice_in_dim(panel, lax.axis_index("ylo") * channels, channels, axis=2)
    rows = row_operand(own)

    split = bins_local // 2
    zs, xs = lax.axis_size("z"), lax.axis_size("x")
    first = ordered_by_position(ring_gather(panel[:split], "x", 3), "x", 0)
    second = ordered_by_position(ring_gather(panel[split:], "z", 3), "z", 0)
    first, second = lax.optimization_barrier((first, second))
    shape = (xs, split, 2, pairs, channels, groups * win_local)
    first = [jnp.transpose(p.reshape(shape), (1, 2, 3, 0, 4, 5)) for p in ring_gather(first, "z", 4)]
    second = [jnp.transpose(p.reshape(shape), (1, 2, 0, 3, 4, 5)) for p in ring_gather(second, "x", 4)]
    first = ordered_by_position(first, "z", 2)
    second = ordered_by_position(second, "x", 4)
    columns = zs * pairs * xs * channels
    halves = []
    for part, block in ((rows[:split], first), (rows[split:], second)):
        block = block.reshape(split, 2, columns, groups * win_local)
        halves.append(
            jnp.einsum("fqipw,fpjw->fqij", part, block, preferred_element_type=jnp.float32)
        )
    return jnp.concatenate(halves, axis=0)


def solution(mesh):
    sizes = dict(zip(mesh.axis_names, mesh.devices.shape))
    chan, freq = sizes["chan"], sizes["freq"]
    devices = mesh.devices.reshape(chan // 8, 2, 4, freq // 2, 2)
    grid = Mesh(devices, ("z", "ylo", "x", "yhi", "core"))
    chan_axes = ("z", "ylo", "x")
    freq_axes = ("yhi", "core")
    return jax.shard_map(
        per_device,
        mesh=grid,
        in_specs=(P(chan_axes, freq_axes, None), P(chan_axes), P(), P(), P(chan_axes)),
        out_specs=P(freq_axes, None, chan_axes, None),
        check_vma=False,
    )
```

```python
import math

import jax
import jax.numpy as jnp
from jax import lax
from jax.sharding import Mesh, PartitionSpec as P

CLIP_FACTOR = 2.0


def dft_table(freq_bins, length):
    samples = jnp.arange(length, dtype=jnp.int32)
    phase_index = samples[:, None] * freq_bins[None, :] % length
    angle = phase_index.astype(jnp.float32) * (2.0 * math.pi / length)
    taper = 0.5 - 0.5 * jnp.cos(samples.astype(jnp.float32) * (2.0 * math.pi / length))
    cosine = taper[:, None] * jnp.cos(angle)
    sine = -taper[:, None] * jnp.sin(angle)
    stacked = jnp.stack([cosine, sine], axis=2)
    return stacked.reshape(length, 2 * freq_bins.shape[0]).astype(jnp.bfloat16)


def clip_scales(mad_index, mad_table):
    entries = jnp.arange(mad_table.shape[0], dtype=jnp.int32)
    matches = mad_index[:, None] == entries[None, :]
    return jnp.sum(jnp.where(matches, mad_table[None, :], 0.0), axis=1)


def row_operand(panel):
    first, second = panel[:, 0], panel[:, 1]
    real_rows = jnp.stack([first, second], axis=2)
    imag_rows = jnp.stack([second, -first], axis=2)
    return jnp.stack([real_rows, imag_rows], axis=1)


def shifted(block, axis, distance):
    size = lax.axis_size(axis)
    return lax.ppermute(block, axis, [((i + distance) % size, i) for i in range(size)])


def ring_gather(block, axis, split_axis):
    ahead = shifted(block, axis, 1)
    behind = shifted(block, axis, -1)
    half = block.shape[split_axis] // 2
    far_a = shifted(lax.slice_in_dim(ahead, 0, half, axis=split_axis), axis, 1)
    far_b = shifted(lax.slice_in_dim(behind, half, 2 * half, axis=split_axis), axis, -1)
    far = jnp.concatenate([far_a, far_b], axis=split_axis)
    return [block, ahead, far, behind]


def ordered_by_position(slots, axis, stack_axis):
    size = len(slots)

    def arrangement(at):
        return lambda *blocks: jnp.stack(
            [blocks[(k - at) % size] for k in range(size)], axis=stack_axis
        )

    return lax.switch(lax.axis_index(axis), [arrangement(at) for at in range(size)], *slots)


def per_device(strain, mad_index, mad_table, freq_bins, valid_count):
    channels, win_local, length = strain.shape
    bin_count = freq_bins.shape[0]
    limits = (clip_scales(mad_index, mad_table) * CLIP_FACTOR)[:, None, None]
    clipped = jnp.clip(strain.astype(jnp.float32), -limits, limits).astype(jnp.bfloat16)
    table = dft_table(freq_bins, length)
    flat_rows = clipped.reshape(channels * win_local, length)
    spectrum = lax.dot_general(
        table, flat_rows, (((0,), (1,)), ((), ())), preferred_element_type=jnp.float32
    )
    freq_index = lax.axis_index("yhi") * lax.axis_size("core") + lax.axis_index("core")
    window_ids = freq_index * win_local + jnp.arange(win_local, dtype=jnp.int32)
    counts = valid_count.astype(jnp.float32)
    weights = jnp.where(
        window_ids[None, :] < valid_count[:, None], 1.0 / jnp.sqrt(counts)[:, None], 0.0
    )
    weighted = (spectrum * weights.reshape(1, channels * win_local)).astype(jnp.bfloat16)
    groups = lax.axis_size("yhi") * lax.axis_size("core")
    pairs = lax.axis_size("ylo")
    bins_local = bin_count // groups
    weighted = weighted.reshape(groups, bins_local, 2, channels, win_local)
    outgoing = jnp.broadcast_to(weighted[None], (pairs,) + weighted.shape)
    outgoing = outgoing.reshape((pairs * groups,) + weighted.shape[1:])
    incoming = lax.all_to_all(outgoing, ("ylo", "yhi", "core"), 0, 0, tiled=True)
    incoming = incoming.reshape(pairs, groups, bins_local, 2, channels, win_local)
    panel = jnp.transpose(incoming, (2, 3, 0, 4, 1, 5)).reshape(
        bins_local, 2, pairs * channels, groups * win_local
    )
    own = lax.dynamic_slice_in_dim(panel, lax.axis_index("ylo") * channels, channels, axis=2)
    rows = row_operand(own)

    split = bins_local // 2
    zs, xs = lax.axis_size("z"), lax.axis_size("x")
    first = ordered_by_position(ring_gather(panel[:split], "x", 3), "x", 0)
    second = ordered_by_position(ring_gather(panel[split:], "z", 3), "z", 0)
    first, second = lax.optimization_barrier((first, second))
    shape = (xs, split, 2, pairs, channels, groups * win_local)
    width = pairs * channels * xs

    def products(part, block, order):
        block = jnp.transpose(block.reshape(shape), order).reshape(split, 2, width, -1)
        return jnp.einsum("fqipw,fpjw->fqij", part, block, preferred_element_type=jnp.float32)

    by_z = [products(rows[:split], p, (1, 2, 3, 0, 4, 5)) for p in ring_gather(first, "z", 4)]
    by_x = [products(rows[split:], p, (1, 2, 0, 3, 4, 5)) for p in ring_gather(second, "x", 4)]

    def arrangement(at_z, at_x):
        def build(*blocks):
            low = jnp.concatenate([blocks[(k - at_z) % zs] for k in range(zs)], axis=3)
            high = jnp.stack(
                [blocks[xs + (k - at_x) % xs].reshape(split, 2, channels, zs, pairs, channels) for k in range(xs)],
                axis=5,
            ).reshape(low.shape)
            return jnp.concatenate([low, high], axis=0)

        return build

    branches = [arrangement(at_z, at_x) for at_z in range(zs) for at_x in range(xs)]
    return lax.switch(lax.axis_index("z") * xs + lax.axis_index("x"), branches, *by_z, *by_x)


def solution(mesh):
    sizes = dict(zip(mesh.axis_names, mesh.devices.shape))
    chan, freq = sizes["chan"], sizes["freq"]
    devices = mesh.devices.reshape(chan // 8, 2, 4, freq // 2, 2)
    grid = Mesh(devices, ("z", "ylo", "x", "yhi", "core"))
    chan_axes = ("z", "ylo", "x")
    freq_axes = ("yhi", "core")
    return jax.shard_map(
        per_device,
        mesh=grid,
        in_specs=(P(chan_axes, freq_axes, None), P(chan_axes), P(), P(), P(chan_axes)),
        out_specs=P(freq_axes, None, chan_axes, None),
        check_vma=False,
    )
```

```python
import math

import jax
import jax.numpy as jnp
from jax import lax
from jax.sharding import Mesh, PartitionSpec as P

CLIP_FACTOR = 2.0


def dft_table(freq_bins, length):
    samples = jnp.arange(length, dtype=jnp.int32)
    phase_index = samples[:, None] * freq_bins[None, :] % length
    angle = phase_index.astype(jnp.float32) * (2.0 * math.pi / length)
    taper = 0.5 - 0.5 * jnp.cos(samples.astype(jnp.float32) * (2.0 * math.pi / length))
    cosine = taper[:, None] * jnp.cos(angle)
    sine = -taper[:, None] * jnp.sin(angle)
    stacked = jnp.stack([cosine, sine], axis=2)
    return stacked.reshape(length, 2 * freq_bins.shape[0]).astype(jnp.bfloat16)


def clip_scales(mad_index, mad_table):
    entries = jnp.arange(mad_table.shape[0], dtype=jnp.int32)
    matches = mad_index[:, None] == entries[None, :]
    return jnp.sum(jnp.where(matches, mad_table[None, :], 0.0), axis=1)


def row_operand(panel):
    first, second = panel[:, 0], panel[:, 1]
    real_rows = jnp.stack([first, second], axis=2)
    imag_rows = jnp.stack([second, -first], axis=2)
    return jnp.stack([real_rows, imag_rows], axis=1)


def shifted(block, axis, distance):
    size = lax.axis_size(axis)
    return lax.ppermute(block, axis, [((i + distance) % size, i) for i in range(size)])


def ring_gather(block, axis, split_axis):
    ahead = shifted(block, axis, 1)
    behind = shifted(block, axis, -1)
    half = block.shape[split_axis] // 2
    far_a = shifted(lax.slice_in_dim(ahead, 0, half, axis=split_axis), axis, 1)
    far_b = shifted(lax.slice_in_dim(behind, half, 2 * half, axis=split_axis), axis, -1)
    far = jnp.concatenate([far_a, far_b], axis=split_axis)
    return [block, ahead, far, behind]


def ordered_by_position(slots, axis, stack_axis):
    size = len(slots)

    def arrangement(at):
        return lambda *blocks: jnp.stack(
            [blocks[(k - at) % size] for k in range(size)], axis=stack_axis
        )

    return lax.switch(lax.axis_index(axis), [arrangement(at) for at in range(size)], *slots)


def per_device(strain, mad_index, mad_table, freq_bins, valid_count):
    channels, win_local, length = strain.shape
    bin_count = freq_bins.shape[0]
    limits = (clip_scales(mad_index, mad_table) * CLIP_FACTOR)[:, None, None]
    clipped = jnp.clip(strain.astype(jnp.float32), -limits, limits).astype(jnp.bfloat16)
    table = dft_table(freq_bins, length)
    flat_rows = clipped.reshape(channels * win_local, length)
    spectrum = lax.dot_general(
        table, flat_rows, (((0,), (1,)), ((), ())), preferred_element_type=jnp.float32
    )
    freq_index = lax.axis_index("yhi") * lax.axis_size("core") + lax.axis_index("core")
    window_ids = freq_index * win_local + jnp.arange(win_local, dtype=jnp.int32)
    counts = valid_count.astype(jnp.float32)
    weights = jnp.where(
        window_ids[None, :] < valid_count[:, None], 1.0 / jnp.sqrt(counts)[:, None], 0.0
    )
    weighted = (spectrum * weights.reshape(1, channels * win_local)).astype(jnp.bfloat16)
    groups = lax.axis_size("yhi") * lax.axis_size("core")
    pairs = lax.axis_size("ylo")
    bins_local = bin_count // groups
    weighted = weighted.reshape(groups, bins_local, 2, channels, win_local)
    outgoing = jnp.broadcast_to(weighted[None], (pairs,) + weighted.shape)
    outgoing = outgoing.reshape((pairs * groups,) + weighted.shape[1:])
    incoming = lax.all_to_all(outgoing, ("ylo", "yhi", "core"), 0, 0, tiled=True)
    incoming = incoming.reshape(pairs, groups, bins_local, 2, channels, win_local)
    panel = jnp.transpose(incoming, (2, 3, 0, 4, 1, 5)).reshape(
        bins_local, 2, pairs * channels, groups * win_local
    )
    own = lax.dynamic_slice_in_dim(panel, lax.axis_index("ylo") * channels, channels, axis=2)
    rows = row_operand(own)

    split = bins_local // 2
    zs, xs = lax.axis_size("z"), lax.axis_size("x")
    first = ordered_by_position(ring_gather(panel[:split], "x", 3), "x", 0)
    second = ordered_by_position(ring_gather(panel[split:], "z", 3), "z", 0)
    first, second = lax.optimization_barrier((first, second))
    shape = (xs, split, 2, pairs, channels, groups * win_local)
    width = pairs * channels * xs

    def products(part, block, order):
        block = jnp.transpose(block.reshape(shape), order).reshape(split, 2, width, -1)
        return jnp.einsum("fqipw,fpjw->fqij", part, block, preferred_element_type=jnp.float32)

    by_z = [products(rows[:split], p, (1, 2, 3, 0, 4, 5)) for p in ring_gather(first, "z", 4)]
    second = [jnp.transpose(p.reshape(shape), (1, 2, 0, 3, 4, 5)) for p in ring_gather(second, "x", 4)]
    second = ordered_by_position(second, "x", 4).reshape(split, 2, width * zs, -1)
    high = jnp.einsum(
        "fqipw,fpjw->fqij", rows[split:], second, preferred_element_type=jnp.float32
    )

    def arrangement(at):
        def build(high, *blocks):
            low = jnp.concatenate([blocks[(k - at) % zs] for k in range(zs)], axis=3)
            return jnp.concatenate([low, high], axis=0)

        return build

    branches = [arrangement(at) for at in range(zs)]
    return lax.switch(lax.axis_index("z"), branches, high, *by_z)


def solution(mesh):
    sizes = dict(zip(mesh.axis_names, mesh.devices.shape))
    chan, freq = sizes["chan"], sizes["freq"]
    devices = mesh.devices.reshape(chan // 8, 2, 4, freq // 2, 2)
    grid = Mesh(devices, ("z", "ylo", "x", "yhi", "core"))
    chan_axes = ("z", "ylo", "x")
    freq_axes = ("yhi", "core")
    return jax.shard_map(
        per_device,
        mesh=grid,
        in_specs=(P(chan_axes, freq_axes, None), P(chan_axes), P(), P(), P(chan_axes)),
        out_specs=P(freq_axes, None, chan_axes, None),
        check_vma=False,
    )
```

```python
import math

import jax
import jax.numpy as jnp
from jax import lax
from jax.sharding import Mesh, PartitionSpec as P

CLIP_FACTOR = 2.0


def dft_table(freq_bins, length):
    samples = jnp.arange(length, dtype=jnp.int32)
    phase_index = samples[:, None] * freq_bins[None, :] % length
    angle = phase_index.astype(jnp.float32) * (2.0 * math.pi / length)
    taper = 0.5 - 0.5 * jnp.cos(samples.astype(jnp.float32) * (2.0 * math.pi / length))
    cosine = taper[:, None] * jnp.cos(angle)
    sine = -taper[:, None] * jnp.sin(angle)
    stacked = jnp.stack([cosine, sine], axis=2)
    return stacked.reshape(length, 2 * freq_bins.shape[0]).astype(jnp.bfloat16)


def clip_scales(mad_index, mad_table):
    entries = jnp.arange(mad_table.shape[0], dtype=jnp.int32)
    matches = mad_index[:, None] == entries[None, :]
    return jnp.sum(jnp.where(matches, mad_table[None, :], 0.0), axis=1)


def row_operand(panel):
    first, second = panel[:, 0], panel[:, 1]
    real_rows = jnp.stack([first, second], axis=2)
    imag_rows = jnp.stack([second, -first], axis=2)
    return jnp.stack([real_rows, imag_rows], axis=1)


def shifted(block, axis, distance):
    size = lax.axis_size(axis)
    return lax.ppermute(block, axis, [((i + distance) % size, i) for i in range(size)])


def ring_gather(block, axis, split_axis):
    ahead = shifted(block, axis, 1)
    behind = shifted(block, axis, -1)
    half = block.shape[split_axis] // 2
    far_a = shifted(lax.slice_in_dim(ahead, 0, half, axis=split_axis), axis, 1)
    far_b = shifted(lax.slice_in_dim(behind, half, 2 * half, axis=split_axis), axis, -1)
    far = jnp.concatenate([far_a, far_b], axis=split_axis)
    return [block, ahead, far, behind]


def ordered_by_position(slots, axis, stack_axis):
    size = len(slots)

    def arrangement(at):
        return lambda *blocks: jnp.stack(
            [blocks[(k - at) % size] for k in range(size)], axis=stack_axis
        )

    return lax.switch(lax.axis_index(axis), [arrangement(at) for at in range(size)], *slots)


def per_device(strain, mad_index, mad_table, freq_bins, valid_count):
    channels, win_local, length = strain.shape
    bin_count = freq_bins.shape[0]
    limits = (clip_scales(mad_index, mad_table) * CLIP_FACTOR)[:, None, None]
    clipped = jnp.clip(strain.astype(jnp.float32), -limits, limits).astype(jnp.bfloat16)
    table = dft_table(freq_bins, length)
    flat_rows = clipped.reshape(channels * win_local, length)
    spectrum = lax.dot_general(
        table, flat_rows, (((0,), (1,)), ((), ())), preferred_element_type=jnp.float32
    )
    freq_index = lax.axis_index("yhi") * lax.axis_size("core") + lax.axis_index("core")
    window_ids = freq_index * win_local + jnp.arange(win_local, dtype=jnp.int32)
    counts = valid_count.astype(jnp.float32)
    weights = jnp.where(
        window_ids[None, :] < valid_count[:, None], 1.0 / jnp.sqrt(counts)[:, None], 0.0
    )
    weighted = (spectrum * weights.reshape(1, channels * win_local)).astype(jnp.bfloat16)
    groups = lax.axis_size("yhi") * lax.axis_size("core")
    pairs = lax.axis_size("ylo")
    bins_local = bin_count // groups
    weighted = weighted.reshape(groups, bins_local, 2, channels, win_local)
    outgoing = jnp.broadcast_to(weighted[None], (pairs,) + weighted.shape)
    outgoing = outgoing.reshape((pairs * groups,) + weighted.shape[1:])
    incoming = lax.all_to_all(outgoing, ("ylo", "yhi", "core"), 0, 0, tiled=True)
    incoming = incoming.reshape(pairs, groups, bins_local, 2, channels, win_local)
    panel = jnp.transpose(incoming, (2, 3, 0, 4, 1, 5)).reshape(
        bins_local, 2, pairs * channels, groups * win_local
    )
    own = lax.dynamic_slice_in_dim(panel, lax.axis_index("ylo") * channels, channels, axis=2)
    rows = row_operand(own)

    split = (bins_local * 9) // 16
    zs, xs = lax.axis_size("z"), lax.axis_size("x")
    first = ordered_by_position(ring_gather(panel[:split], "x", 3), "x", 0)
    second = ordered_by_position(ring_gather(panel[split:], "z", 3), "z", 0)
    first, second = lax.optimization_barrier((first, second))
    shape = (xs, -1, 2, pairs, channels, groups * win_local)
    width = pairs * channels * xs

    def products(part, block, order):
        block = jnp.transpose(block.reshape(shape), order).reshape(-1, 2, width, groups * win_local)
        return jnp.einsum("fqipw,fpjw->fqij", part, block, preferred_element_type=jnp.float32)

    by_z = [products(rows[:split], p, (1, 2, 3, 0, 4, 5)) for p in ring_gather(first, "z", 4)]
    second = [jnp.transpose(p.reshape(shape), (1, 2, 0, 3, 4, 5)) for p in ring_gather(second, "x", 4)]
    second = ordered_by_position(second, "x", 4).reshape(-1, 2, width * zs, groups * win_local)
    high = jnp.einsum(
        "fqipw,fpjw->fqij", rows[split:], second, preferred_element_type=jnp.float32
    )

    def arrangement(at):
        def build(high, *blocks):
            low = jnp.concatenate([blocks[(k - at) % zs] for k in range(zs)], axis=3)
            return jnp.concatenate([low, high], axis=0)

        return build

    branches = [arrangement(at) for at in range(zs)]
    return lax.switch(lax.axis_index("z"), branches, high, *by_z)


def solution(mesh):
    sizes = dict(zip(mesh.axis_names, mesh.devices.shape))
    chan, freq = sizes["chan"], sizes["freq"]
    devices = mesh.devices.reshape(chan // 8, 2, 4, freq // 2, 2)
    grid = Mesh(devices, ("z", "ylo", "x", "yhi", "core"))
    chan_axes = ("z", "ylo", "x")
    freq_axes = ("yhi", "core")
    return jax.shard_map(
        per_device,
        mesh=grid,
        in_specs=(P(chan_axes, freq_axes, None), P(chan_axes), P(), P(), P(chan_axes)),
        out_specs=P(freq_axes, None, chan_axes, None),
        check_vma=False,
    )
```

```python
import math

import jax
import jax.numpy as jnp
from jax import lax
from jax.sharding import Mesh, PartitionSpec as P

CLIP_FACTOR = 2.0


def dft_table(freq_bins, length):
    samples = jnp.arange(length, dtype=jnp.int32)
    phase_index = samples[:, None] * freq_bins[None, :] % length
    angle = phase_index.astype(jnp.float32) * (2.0 * math.pi / length)
    taper = 0.5 - 0.5 * jnp.cos(samples.astype(jnp.float32) * (2.0 * math.pi / length))
    cosine = taper[:, None] * jnp.cos(angle)
    sine = -taper[:, None] * jnp.sin(angle)
    stacked = jnp.stack([cosine, sine], axis=2)
    return stacked.reshape(length, 2 * freq_bins.shape[0]).astype(jnp.bfloat16)


def clip_scales(mad_index, mad_table):
    entries = jnp.arange(mad_table.shape[0], dtype=jnp.int32)
    matches = mad_index[:, None] == entries[None, :]
    return jnp.sum(jnp.where(matches, mad_table[None, :], 0.0), axis=1)


def row_operand(panel):
    first, second = panel[:, 0], panel[:, 1]
    real_rows = jnp.stack([first, second], axis=2)
    imag_rows = jnp.stack([second, -first], axis=2)
    return jnp.stack([real_rows, imag_rows], axis=1)


def shifted(block, axis, distance):
    size = lax.axis_size(axis)
    return lax.ppermute(block, axis, [((i + distance) % size, i) for i in range(size)])


def ring_gather(block, axis, split_axis):
    ahead = shifted(block, axis, 1)
    behind = shifted(block, axis, -1)
    half = block.shape[split_axis] // 2
    far_a = shifted(lax.slice_in_dim(ahead, 0, half, axis=split_axis), axis, 1)
    far_b = shifted(lax.slice_in_dim(behind, half, 2 * half, axis=split_axis), axis, -1)
    far = jnp.concatenate([far_a, far_b], axis=split_axis)
    return [block, ahead, far, behind]


def ordered_by_position(slots, axis, stack_axis):
    size = len(slots)

    def arrangement(at):
        return lambda *blocks: jnp.stack(
            [blocks[(k - at) % size] for k in range(size)], axis=stack_axis
        )

    return lax.switch(lax.axis_index(axis), [arrangement(at) for at in range(size)], *slots)


def per_device(strain, mad_index, mad_table, freq_bins, valid_count):
    channels, win_local, length = strain.shape
    bin_count = freq_bins.shape[0]
    limits = (clip_scales(mad_index, mad_table) * CLIP_FACTOR)[:, None, None]
    clipped = jnp.clip(strain.astype(jnp.float32), -limits, limits).astype(jnp.bfloat16)
    table = dft_table(freq_bins, length)
    flat_rows = clipped.reshape(channels * win_local, length)
    spectrum = lax.dot_general(
        table, flat_rows, (((0,), (1,)), ((), ())), preferred_element_type=jnp.float32
    )
    freq_index = lax.axis_index("yhi") * lax.axis_size("core") + lax.axis_index("core")
    window_ids = freq_index * win_local + jnp.arange(win_local, dtype=jnp.int32)
    counts = valid_count.astype(jnp.float32)
    weights = jnp.where(
        window_ids[None, :] < valid_count[:, None], 1.0 / jnp.sqrt(counts)[:, None], 0.0
    )
    weighted = (spectrum * weights.reshape(1, channels * win_local)).astype(jnp.bfloat16)
    groups = lax.axis_size("yhi") * lax.axis_size("core")
    pairs = lax.axis_size("ylo")
    bins_local = bin_count // groups
    weighted = weighted.reshape(groups, bins_local, 2, channels, win_local)
    outgoing = jnp.broadcast_to(weighted[None], (pairs,) + weighted.shape)
    outgoing = outgoing.reshape((pairs * groups,) + weighted.shape[1:])
    incoming = lax.all_to_all(outgoing, ("ylo", "yhi", "core"), 0, 0, tiled=True)
    incoming = incoming.reshape(pairs, groups, bins_local, 2, channels, win_local)
    panel = jnp.transpose(incoming, (2, 3, 0, 4, 1, 5)).reshape(
        bins_local, 2, pairs * channels, groups * win_local
    )
    own = lax.dynamic_slice_in_dim(panel, lax.axis_index("ylo") * channels, channels, axis=2)
    rows = row_operand(own)

    split = (bins_local * 9) // 16
    zs, xs = lax.axis_size("z"), lax.axis_size("x")
    first = ordered_by_position(ring_gather(panel[:split], "x", 3), "x", 0)
    second = ordered_by_position(ring_gather(panel[split:], "z", 3), "z", 0)
    first, second, rows = lax.optimization_barrier((first, second, rows))
    shape = (xs, -1, 2, pairs, channels, groups * win_local)
    width = pairs * channels * xs

    def products(part, block, order):
        block = jnp.transpose(block.reshape(shape), order).reshape(-1, 2, width, groups * win_local)
        return jnp.einsum("fqipw,fpjw->fqij", part, block, preferred_element_type=jnp.float32)

    by_z = [products(rows[:split], p, (1, 2, 3, 0, 4, 5)) for p in ring_gather(first, "z", 4)]
    second = [jnp.transpose(p.reshape(shape), (1, 2, 0, 3, 4, 5)) for p in ring_gather(second, "x", 4)]
    second = ordered_by_position(second, "x", 4).reshape(-1, 2, width * zs, groups * win_local)
    high = jnp.einsum(
        "fqipw,fpjw->fqij", rows[split:], second, preferred_element_type=jnp.float32
    )

    def arrangement(at):
        def build(high, *blocks):
            low = jnp.concatenate([blocks[(k - at) % zs] for k in range(zs)], axis=3)
            return jnp.concatenate([low, high], axis=0)

        return build

    branches = [arrangement(at) for at in range(zs)]
    return lax.switch(lax.axis_index("z"), branches, high, *by_z)


def solution(mesh):
    sizes = dict(zip(mesh.axis_names, mesh.devices.shape))
    chan, freq = sizes["chan"], sizes["freq"]
    devices = mesh.devices.reshape(chan // 8, 2, 4, freq // 2, 2)
    grid = Mesh(devices, ("z", "ylo", "x", "yhi", "core"))
    chan_axes = ("z", "ylo", "x")
    freq_axes = ("yhi", "core")
    return jax.shard_map(
        per_device,
        mesh=grid,
        in_specs=(P(chan_axes, freq_axes, None), P(chan_axes), P(), P(), P(chan_axes)),
        out_specs=P(freq_axes, None, chan_axes, None),
        check_vma=False,
    )
```

```python
import math

import jax
import jax.numpy as jnp
from jax import lax
from jax.sharding import Mesh, PartitionSpec as P

CLIP_FACTOR = 2.0


def dft_table(freq_bins, length):
    samples = jnp.arange(length, dtype=jnp.int32)
    phase_index = samples[:, None] * freq_bins[None, :] % length
    angle = phase_index.astype(jnp.float32) * (2.0 * math.pi / length)
    taper = 0.5 - 0.5 * jnp.cos(samples.astype(jnp.float32) * (2.0 * math.pi / length))
    cosine = taper[:, None] * jnp.cos(angle)
    sine = -taper[:, None] * jnp.sin(angle)
    stacked = jnp.stack([cosine, sine], axis=2)
    return stacked.reshape(length, 2 * freq_bins.shape[0]).astype(jnp.bfloat16)


def clip_scales(mad_index, mad_table):
    entries = jnp.arange(mad_table.shape[0], dtype=jnp.int32)
    matches = mad_index[:, None] == entries[None, :]
    return jnp.sum(jnp.where(matches, mad_table[None, :], 0.0), axis=1)


def row_operand(panel):
    first, second = panel[:, 0], panel[:, 1]
    real_rows = jnp.stack([first, second], axis=2)
    imag_rows = jnp.stack([second, -first], axis=2)
    return jnp.stack([real_rows, imag_rows], axis=1)


def shifted(block, axis, distance):
    size = lax.axis_size(axis)
    return lax.ppermute(block, axis, [((i + distance) % size, i) for i in range(size)])


def ring_gather(block, axis, split_axis):
    ahead = shifted(block, axis, 1)
    behind = shifted(block, axis, -1)
    half = block.shape[split_axis] // 2
    far_a = shifted(lax.slice_in_dim(ahead, 0, half, axis=split_axis), axis, 1)
    far_b = shifted(lax.slice_in_dim(behind, half, 2 * half, axis=split_axis), axis, -1)
    far = jnp.concatenate([far_a, far_b], axis=split_axis)
    return [block, ahead, far, behind]


def ordered_by_position(slots, axis, stack_axis):
    size = len(slots)

    def arrangement(at):
        return lambda *blocks: jnp.stack(
            [blocks[(k - at) % size] for k in range(size)], axis=stack_axis
        )

    return lax.switch(lax.axis_index(axis), [arrangement(at) for at in range(size)], *slots)


def per_device(strain, mad_index, mad_table, freq_bins, valid_count):
    channels, win_local, length = strain.shape
    bin_count = freq_bins.shape[0]
    limits = (clip_scales(mad_index, mad_table) * CLIP_FACTOR)[:, None, None]
    clipped = jnp.clip(strain.astype(jnp.float32), -limits, limits).astype(jnp.bfloat16)
    table = dft_table(freq_bins, length)
    flat_rows = clipped.reshape(channels * win_local, length)
    spectrum = lax.dot_general(
        table, flat_rows, (((0,), (1,)), ((), ())), preferred_element_type=jnp.float32
    )
    freq_index = lax.axis_index("yhi") * lax.axis_size("core") + lax.axis_index("core")
    window_ids = freq_index * win_local + jnp.arange(win_local, dtype=jnp.int32)
    counts = valid_count.astype(jnp.float32)
    weights = jnp.where(
        window_ids[None, :] < valid_count[:, None], 1.0 / jnp.sqrt(counts)[:, None], 0.0
    )
    weighted = (spectrum * weights.reshape(1, channels * win_local)).astype(jnp.bfloat16)
    groups = lax.axis_size("yhi") * lax.axis_size("core")
    pairs = lax.axis_size("ylo")
    bins_local = bin_count // groups
    weighted = weighted.reshape(groups, bins_local, 2, channels, win_local)

    def exchanged(part):
        outgoing = jnp.broadcast_to(part[None], (pairs,) + part.shape)
        outgoing = outgoing.reshape((pairs * groups,) + part.shape[1:])
        incoming = lax.all_to_all(outgoing, ("ylo", "yhi", "core"), 0, 0, tiled=True)
        incoming = incoming.reshape((pairs,) + part.shape)
        panel = jnp.transpose(incoming, (2, 3, 0, 4, 1, 5)).reshape(
            part.shape[1], 2, pairs * channels, groups * win_local
        )
        own = lax.dynamic_slice_in_dim(panel, lax.axis_index("ylo") * channels, channels, axis=2)
        return panel, row_operand(own)

    split = (bins_local * 9) // 16
    zs, xs = lax.axis_size("z"), lax.axis_size("x")
    panel, rows_low = exchanged(weighted[:, :split])
    first = ordered_by_position(ring_gather(panel, "x", 3), "x", 0)
    panel, rows_high = exchanged(weighted[:, split:])
    second = ordered_by_position(ring_gather(panel, "z", 3), "z", 0)
    first, second, rows_low, rows_high = lax.optimization_barrier(
        (first, second, rows_low, rows_high)
    )
    shape = (xs, -1, 2, pairs, channels, groups * win_local)
    width = pairs * channels * xs

    def products(part, block, order):
        block = jnp.transpose(block.reshape(shape), order).reshape(-1, 2, width, groups * win_local)
        return jnp.einsum("fqipw,fpjw->fqij", part, block, preferred_element_type=jnp.float32)

    by_z = [products(rows_low, p, (1, 2, 3, 0, 4, 5)) for p in ring_gather(first, "z", 4)]
    second = [jnp.transpose(p.reshape(shape), (1, 2, 0, 3, 4, 5)) for p in ring_gather(second, "x", 4)]
    second = ordered_by_position(second, "x", 4).reshape(-1, 2, width * zs, groups * win_local)
    high = jnp.einsum(
        "fqipw,fpjw->fqij", rows_high, second, preferred_element_type=jnp.float32
    )

    def arrangement(at):
        def build(high, *blocks):
            low = jnp.concatenate([blocks[(k - at) % zs] for k in range(zs)], axis=3)
            return jnp.concatenate([low, high], axis=0)

        return build

    branches = [arrangement(at) for at in range(zs)]
    return lax.switch(lax.axis_index("z"), branches, high, *by_z)


def solution(mesh):
    sizes = dict(zip(mesh.axis_names, mesh.devices.shape))
    chan, freq = sizes["chan"], sizes["freq"]
    devices = mesh.devices.reshape(chan // 8, 2, 4, freq // 2, 2)
    grid = Mesh(devices, ("z", "ylo", "x", "yhi", "core"))
    chan_axes = ("z", "ylo", "x")
    freq_axes = ("yhi", "core")
    return jax.shard_map(
        per_device,
        mesh=grid,
        in_specs=(P(chan_axes, freq_axes, None), P(chan_axes), P(), P(), P(chan_axes)),
        out_specs=P(freq_axes, None, chan_axes, None),
        check_vma=False,
    )
```

```python
import math

import jax
import jax.numpy as jnp
from jax import lax
from jax.sharding import Mesh, PartitionSpec as P

CLIP_FACTOR = 2.0


def dft_table(freq_bins, length):
    samples = jnp.arange(length, dtype=jnp.int32)
    phase_index = samples[:, None] * freq_bins[None, :] % length
    angle = phase_index.astype(jnp.float32) * (2.0 * math.pi / length)
    taper = 0.5 - 0.5 * jnp.cos(samples.astype(jnp.float32) * (2.0 * math.pi / length))
    cosine = taper[:, None] * jnp.cos(angle)
    sine = -taper[:, None] * jnp.sin(angle)
    stacked = jnp.stack([cosine, sine], axis=2)
    return stacked.reshape(length, 2 * freq_bins.shape[0]).astype(jnp.bfloat16)


def clip_scales(mad_index, mad_table):
    entries = jnp.arange(mad_table.shape[0], dtype=jnp.int32)
    matches = mad_index[:, None] == entries[None, :]
    return jnp.sum(jnp.where(matches, mad_table[None, :], 0.0), axis=1)


def row_operand(panel):
    first, second = panel[:, 0], panel[:, 1]
    real_rows = jnp.stack([first, second], axis=2)
    imag_rows = jnp.stack([second, -first], axis=2)
    return jnp.stack([real_rows, imag_rows], axis=1)


def shifted(block, axis, distance):
    size = lax.axis_size(axis)
    return lax.ppermute(block, axis, [((i + distance) % size, i) for i in range(size)])


def ring_gather(block, axis, split_axis):
    ahead = shifted(block, axis, 1)
    behind = shifted(block, axis, -1)
    half = block.shape[split_axis] // 2
    far_a = shifted(lax.slice_in_dim(ahead, 0, half, axis=split_axis), axis, 1)
    far_b = shifted(lax.slice_in_dim(behind, half, 2 * half, axis=split_axis), axis, -1)
    far = jnp.concatenate([far_a, far_b], axis=split_axis)
    return [block, ahead, far, behind]


def ordered_by_position(slots, axis, stack_axis):
    size = len(slots)

    def arrangement(at):
        return lambda *blocks: jnp.stack(
            [blocks[(k - at) % size] for k in range(size)], axis=stack_axis
        )

    return lax.switch(lax.axis_index(axis), [arrangement(at) for at in range(size)], *slots)


def per_device(strain, mad_index, mad_table, freq_bins, valid_count):
    channels, win_local, length = strain.shape
    bin_count = freq_bins.shape[0]
    limits = (clip_scales(mad_index, mad_table) * CLIP_FACTOR)[:, None, None]
    bound = limits.astype(strain.dtype)
    clipped = jnp.minimum(jnp.maximum(strain, -bound), bound)
    table = dft_table(freq_bins, length)
    flat_rows = clipped.reshape(channels * win_local, length)
    spectrum = lax.dot_general(
        table, flat_rows, (((0,), (1,)), ((), ())), preferred_element_type=jnp.float32
    )
    freq_index = lax.axis_index("yhi") * lax.axis_size("core") + lax.axis_index("core")
    window_ids = freq_index * win_local + jnp.arange(win_local, dtype=jnp.int32)
    counts = valid_count.astype(jnp.float32)
    weights = jnp.where(
        window_ids[None, :] < valid_count[:, None], 1.0 / jnp.sqrt(counts)[:, None], 0.0
    )
    weighted = (spectrum * weights.reshape(1, channels * win_local)).astype(jnp.bfloat16)
    groups = lax.axis_size("yhi") * lax.axis_size("core")
    pairs = lax.axis_size("ylo")
    bins_local = bin_count // groups
    weighted = weighted.reshape(groups, bins_local, 2, channels, win_local)
    outgoing = jnp.broadcast_to(weighted[None], (pairs,) + weighted.shape)
    outgoing = outgoing.reshape((pairs * groups,) + weighted.shape[1:])
    incoming = lax.all_to_all(outgoing, ("ylo", "yhi", "core"), 0, 0, tiled=True)
    incoming = incoming.reshape(pairs, groups, bins_local, 2, channels, win_local)
    panel = jnp.transpose(incoming, (2, 3, 0, 4, 1, 5)).reshape(
        bins_local, 2, pairs * channels, groups * win_local
    )
    own = lax.dynamic_slice_in_dim(panel, lax.axis_index("ylo") * channels, channels, axis=2)
    rows = row_operand(own)

    split = (bins_local * 9) // 16
    zs, xs = lax.axis_size("z"), lax.axis_size("x")
    first = ordered_by_position(ring_gather(panel[:split], "x", 3), "x", 0)
    second = ordered_by_position(ring_gather(panel[split:], "z", 3), "z", 0)
    first, second, rows = lax.optimization_barrier((first, second, rows))
    shape = (xs, -1, 2, pairs, channels, groups * win_local)
    width = pairs * channels * xs

    def products(part, block, order):
        block = jnp.transpose(block.reshape(shape), order).reshape(-1, 2, width, groups * win_local)
        return jnp.einsum("fqipw,fpjw->fqij", part, block, preferred_element_type=jnp.float32)

    by_z = [products(rows[:split], p, (1, 2, 3, 0, 4, 5)) for p in ring_gather(first, "z", 4)]
    second = [jnp.transpose(p.reshape(shape), (1, 2, 0, 3, 4, 5)) for p in ring_gather(second, "x", 4)]
    second = ordered_by_position(second, "x", 4).reshape(-1, 2, width * zs, groups * win_local)
    high = jnp.einsum(
        "fqipw,fpjw->fqij", rows[split:], second, preferred_element_type=jnp.float32
    )

    def arrangement(at):
        def build(high, *blocks):
            low = jnp.concatenate([blocks[(k - at) % zs] for k in range(zs)], axis=3)
            return jnp.concatenate([low, high], axis=0)

        return build

    branches = [arrangement(at) for at in range(zs)]
    return lax.switch(lax.axis_index("z"), branches, high, *by_z)


def solution(mesh):
    sizes = dict(zip(mesh.axis_names, mesh.devices.shape))
    chan, freq = sizes["chan"], sizes["freq"]
    devices = mesh.devices.reshape(chan // 8, 2, 4, freq // 2, 2)
    grid = Mesh(devices, ("z", "ylo", "x", "yhi", "core"))
    chan_axes = ("z", "ylo", "x")
    freq_axes = ("yhi", "core")
    return jax.shard_map(
        per_device,
        mesh=grid,
        in_specs=(P(chan_axes, freq_axes, None), P(chan_axes), P(), P(), P(chan_axes)),
        out_specs=P(freq_axes, None, chan_axes, None),
        check_vma=False,
    )
```

```python
import math

import jax
import jax.numpy as jnp
from jax import lax
from jax.sharding import Mesh, PartitionSpec as P

CLIP_FACTOR = 2.0


def dft_table(freq_bins, length):
    samples = jnp.arange(length, dtype=jnp.int32)
    phase_index = samples[:, None] * freq_bins[None, :] % length
    angle = phase_index.astype(jnp.float32) * (2.0 * math.pi / length)
    taper = 0.5 - 0.5 * jnp.cos(samples.astype(jnp.float32) * (2.0 * math.pi / length))
    cosine = taper[:, None] * jnp.cos(angle)
    sine = -taper[:, None] * jnp.sin(angle)
    stacked = jnp.stack([cosine, sine], axis=2)
    return stacked.reshape(length, 2 * freq_bins.shape[0]).astype(jnp.bfloat16)


def clip_scales(mad_index, mad_table):
    entries = jnp.arange(mad_table.shape[0], dtype=jnp.int32)
    matches = mad_index[:, None] == entries[None, :]
    return jnp.sum(jnp.where(matches, mad_table[None, :], 0.0), axis=1)


def row_operand(panel):
    first, second = panel[:, 0], panel[:, 1]
    real_rows = jnp.stack([first, second], axis=2)
    imag_rows = jnp.stack([second, -first], axis=2)
    return jnp.stack([real_rows, imag_rows], axis=1)


def shifted(block, axis, distance):
    size = lax.axis_size(axis)
    return lax.ppermute(block, axis, [((i + distance) % size, i) for i in range(size)])


def ring_gather(block, axis, split_axis):
    ahead = shifted(block, axis, 1)
    behind = shifted(block, axis, -1)
    half = block.shape[split_axis] // 2
    far_a = shifted(lax.slice_in_dim(ahead, 0, half, axis=split_axis), axis, 1)
    far_b = shifted(lax.slice_in_dim(behind, half, 2 * half, axis=split_axis), axis, -1)
    far = jnp.concatenate([far_a, far_b], axis=split_axis)
    return [block, ahead, far, behind]


def ordered_by_position(slots, axis, stack_axis):
    size = len(slots)

    def arrangement(at):
        return lambda *blocks: jnp.stack(
            [blocks[(k - at) % size] for k in range(size)], axis=stack_axis
        )

    return lax.switch(lax.axis_index(axis), [arrangement(at) for at in range(size)], *slots)


def per_device(strain, mad_index, mad_table, freq_bins, valid_count):
    channels, win_local, length = strain.shape
    bin_count = freq_bins.shape[0]
    limits = (clip_scales(mad_index, mad_table) * CLIP_FACTOR)[:, None, None]
    bound = limits.astype(strain.dtype)
    clipped = jnp.minimum(jnp.maximum(strain, -bound), bound)
    table = dft_table(freq_bins, length)
    flat_rows = clipped.reshape(channels * win_local, length)
    spectrum = lax.dot_general(
        table, flat_rows, (((0,), (1,)), ((), ())), preferred_element_type=jnp.float32
    )
    freq_index = lax.axis_index("yhi") * lax.axis_size("core") + lax.axis_index("core")
    window_ids = freq_index * win_local + jnp.arange(win_local, dtype=jnp.int32)
    counts = valid_count.astype(jnp.float32)
    weights = jnp.where(
        window_ids[None, :] < valid_count[:, None], 1.0 / jnp.sqrt(counts)[:, None], 0.0
    )
    weighted = (spectrum * weights.reshape(1, channels * win_local)).astype(jnp.bfloat16)
    groups = lax.axis_size("yhi") * lax.axis_size("core")
    pairs = lax.axis_size("ylo")
    bins_local = bin_count // groups
    weighted = weighted.reshape(groups, bins_local * 2, channels * win_local)
    outgoing = jnp.broadcast_to(weighted[None], (pairs,) + weighted.shape)
    outgoing = outgoing.reshape((pairs * groups,) + weighted.shape[1:])
    incoming = lax.all_to_all(outgoing, ("ylo", "yhi", "core"), 0, 0, tiled=True)
    incoming = incoming.reshape(pairs, groups, bins_local, 2, channels, win_local)
    panel = jnp.transpose(incoming, (2, 3, 0, 4, 1, 5)).reshape(
        bins_local, 2, pairs * channels, groups * win_local
    )
    own = lax.dynamic_slice_in_dim(panel, lax.axis_index("ylo") * channels, channels, axis=2)
    rows = row_operand(own)

    split = (bins_local * 9) // 16
    zs, xs = lax.axis_size("z"), lax.axis_size("x")
    first = ordered_by_position(ring_gather(panel[:split], "x", 3), "x", 0)
    second = ordered_by_position(ring_gather(panel[split:], "z", 3), "z", 0)
    first, second, rows = lax.optimization_barrier((first, second, rows))
    shape = (xs, -1, 2, pairs, channels, groups * win_local)
    width = pairs * channels * xs

    def products(part, block, order):
        block = jnp.transpose(block.reshape(shape), order).reshape(-1, 2, width, groups * win_local)
        return jnp.einsum("fqipw,fpjw->fqij", part, block, preferred_element_type=jnp.float32)

    by_z = [products(rows[:split], p, (1, 2, 3, 0, 4, 5)) for p in ring_gather(first, "z", 4)]
    second = [jnp.transpose(p.reshape(shape), (1, 2, 0, 3, 4, 5)) for p in ring_gather(second, "x", 4)]
    second = ordered_by_position(second, "x", 4).reshape(-1, 2, width * zs, groups * win_local)
    high = jnp.einsum(
        "fqipw,fpjw->fqij", rows[split:], second, preferred_element_type=jnp.float32
    )

    def arrangement(at):
        def build(high, *blocks):
            low = jnp.concatenate([blocks[(k - at) % zs] for k in range(zs)], axis=3)
            return jnp.concatenate([low, high], axis=0)

        return build

    branches = [arrangement(at) for at in range(zs)]
    return lax.switch(lax.axis_index("z"), branches, high, *by_z)


def solution(mesh):
    sizes = dict(zip(mesh.axis_names, mesh.devices.shape))
    chan, freq = sizes["chan"], sizes["freq"]
    devices = mesh.devices.reshape(chan // 8, 2, 4, freq // 2, 2)
    grid = Mesh(devices, ("z", "ylo", "x", "yhi", "core"))
    chan_axes = ("z", "ylo", "x")
    freq_axes = ("yhi", "core")
    return jax.shard_map(
        per_device,
        mesh=grid,
        in_specs=(P(chan_axes, freq_axes, None), P(chan_axes), P(), P(), P(chan_axes)),
        out_specs=P(freq_axes, None, chan_axes, None),
        check_vma=False,
    )
```

```python
import math

import jax
import jax.numpy as jnp
from jax import lax
from jax.sharding import Mesh, PartitionSpec as P

CLIP_FACTOR = 2.0


def dft_table(freq_bins, length):
    samples = jnp.arange(length, dtype=jnp.int32)
    phase_index = samples[:, None] * freq_bins[None, :] % length
    angle = phase_index.astype(jnp.float32) * (2.0 * math.pi / length)
    taper = 0.5 - 0.5 * jnp.cos(samples.astype(jnp.float32) * (2.0 * math.pi / length))
    cosine = taper[:, None] * jnp.cos(angle)
    sine = -taper[:, None] * jnp.sin(angle)
    stacked = jnp.stack([cosine, sine], axis=2)
    return stacked.reshape(length, 2 * freq_bins.shape[0]).astype(jnp.bfloat16)


def clip_scales(mad_index, mad_table):
    entries = jnp.arange(mad_table.shape[0], dtype=jnp.int32)
    matches = mad_index[:, None] == entries[None, :]
    return jnp.sum(jnp.where(matches, mad_table[None, :], 0.0), axis=1)


def row_operand(panel):
    first, second = panel[:, 0], panel[:, 1]
    real_rows = jnp.stack([first, second], axis=2)
    imag_rows = jnp.stack([second, -first], axis=2)
    return jnp.stack([real_rows, imag_rows], axis=1)


def shifted(block, axis, distance):
    size = lax.axis_size(axis)
    return lax.ppermute(block, axis, [((i + distance) % size, i) for i in range(size)])


def ring_gather(block, axis, split_axis):
    ahead = shifted(block, axis, 1)
    behind = shifted(block, axis, -1)
    half = block.shape[split_axis] // 2
    far_a = shifted(lax.slice_in_dim(ahead, 0, half, axis=split_axis), axis, 1)
    far_b = shifted(lax.slice_in_dim(behind, half, 2 * half, axis=split_axis), axis, -1)
    far = jnp.concatenate([far_a, far_b], axis=split_axis)
    return [block, ahead, far, behind]


def ordered_by_position(slots, axis, stack_axis):
    size = len(slots)

    def arrangement(at):
        return lambda *blocks: jnp.stack(
            [blocks[(k - at) % size] for k in range(size)], axis=stack_axis
        )

    return lax.switch(lax.axis_index(axis), [arrangement(at) for at in range(size)], *slots)


def per_device(strain, mad_index, mad_table, freq_bins, valid_count):
    channels, win_local, length = strain.shape
    bin_count = freq_bins.shape[0]
    limits = (clip_scales(mad_index, mad_table) * CLIP_FACTOR)[:, None, None]
    bound = limits.astype(strain.dtype)
    clipped = jnp.minimum(jnp.maximum(strain, -bound), bound)
    table = dft_table(freq_bins, length)
    flat_rows = clipped.reshape(channels * win_local, length)
    spectrum = lax.dot_general(
        table, flat_rows, (((0,), (1,)), ((), ())), preferred_element_type=jnp.float32
    )
    freq_index = lax.axis_index("yhi") * lax.axis_size("core") + lax.axis_index("core")
    window_ids = freq_index * win_local + jnp.arange(win_local, dtype=jnp.int32)
    counts = valid_count.astype(jnp.float32)
    weights = jnp.where(
        window_ids[None, :] < valid_count[:, None], 1.0 / jnp.sqrt(counts)[:, None], 0.0
    )
    weighted = (spectrum * weights.reshape(1, channels * win_local)).astype(jnp.bfloat16)
    groups = lax.axis_size("yhi") * lax.axis_size("core")
    pairs = lax.axis_size("ylo")
    bins_local = bin_count // groups
    weighted = weighted.reshape(groups, bins_local * 2, channels * win_local)
    outgoing = jnp.broadcast_to(weighted[None], (pairs,) + weighted.shape)
    outgoing = outgoing.reshape((pairs * groups,) + weighted.shape[1:])
    incoming = lax.all_to_all(outgoing, ("ylo", "yhi", "core"), 0, 0, tiled=True)
    incoming = incoming.reshape(pairs, groups, bins_local, 2, channels, win_local)
    panel = jnp.transpose(incoming, (2, 3, 0, 4, 1, 5)).reshape(
        bins_local, 2, pairs * channels, groups * win_local
    )

    split = (bins_local * 9) // 16
    zs, xs = lax.axis_size("z"), lax.axis_size("x")
    low, high = panel[:split], panel[split:]
    first = ordered_by_position(ring_gather(low, "x", 3), "x", 0)
    second = ordered_by_position(ring_gather(high, "z", 3), "z", 0)
    at = lax.axis_index("ylo") * channels
    rows_low = row_operand(lax.dynamic_slice_in_dim(low, at, channels, axis=2))
    rows_high = row_operand(lax.dynamic_slice_in_dim(high, at, channels, axis=2))
    first, second, rows_low, rows_high = lax.optimization_barrier(
        (first, second, rows_low, rows_high)
    )
    shape = (xs, -1, 2, pairs, channels, groups * win_local)
    width = pairs * channels * xs

    def products(part, block, order):
        block = jnp.transpose(block.reshape(shape), order).reshape(-1, 2, width, groups * win_local)
        return jnp.einsum("fqipw,fpjw->fqij", part, block, preferred_element_type=jnp.float32)

    by_z = [products(rows_low, p, (1, 2, 3, 0, 4, 5)) for p in ring_gather(first, "z", 4)]
    second = [jnp.transpose(p.reshape(shape), (1, 2, 0, 3, 4, 5)) for p in ring_gather(second, "x", 4)]
    second = ordered_by_position(second, "x", 4).reshape(-1, 2, width * zs, groups * win_local)
    high = jnp.einsum(
        "fqipw,fpjw->fqij", rows_high, second, preferred_element_type=jnp.float32
    )

    def arrangement(at):
        def build(high, *blocks):
            low = jnp.concatenate([blocks[(k - at) % zs] for k in range(zs)], axis=3)
            return jnp.concatenate([low, high], axis=0)

        return build

    branches = [arrangement(at) for at in range(zs)]
    return lax.switch(lax.axis_index("z"), branches, high, *by_z)


def solution(mesh):
    sizes = dict(zip(mesh.axis_names, mesh.devices.shape))
    chan, freq = sizes["chan"], sizes["freq"]
    devices = mesh.devices.reshape(chan // 8, 2, 4, freq // 2, 2)
    grid = Mesh(devices, ("z", "ylo", "x", "yhi", "core"))
    chan_axes = ("z", "ylo", "x")
    freq_axes = ("yhi", "core")
    return jax.shard_map(
        per_device,
        mesh=grid,
        in_specs=(P(chan_axes, freq_axes, None), P(chan_axes), P(), P(), P(chan_axes)),
        out_specs=P(freq_axes, None, chan_axes, None),
        check_vma=False,
    )
```

```python
import math

import jax
import jax.numpy as jnp
from jax import lax
from jax.sharding import Mesh, PartitionSpec as P

CLIP_FACTOR = 2.0


def dft_table(freq_bins, length):
    samples = jnp.arange(length, dtype=jnp.int32)
    phase_index = samples[:, None] * freq_bins[None, :] % length
    angle = phase_index.astype(jnp.float32) * (2.0 * math.pi / length)
    taper = 0.5 - 0.5 * jnp.cos(samples.astype(jnp.float32) * (2.0 * math.pi / length))
    cosine = taper[:, None] * jnp.cos(angle)
    sine = -taper[:, None] * jnp.sin(angle)
    stacked = jnp.stack([cosine, sine], axis=2)
    return stacked.reshape(length, 2 * freq_bins.shape[0]).astype(jnp.bfloat16)


def clip_scales(mad_index, mad_table):
    entries = jnp.arange(mad_table.shape[0], dtype=jnp.int32)
    matches = mad_index[:, None] == entries[None, :]
    return jnp.sum(jnp.where(matches, mad_table[None, :], 0.0), axis=1)


def row_operand(panel):
    first, second = panel[:, 0], panel[:, 1]
    real_rows = jnp.stack([first, second], axis=2)
    imag_rows = jnp.stack([second, -first], axis=2)
    return jnp.stack([real_rows, imag_rows], axis=1)


def shifted(block, axis, distance):
    size = lax.axis_size(axis)
    return lax.ppermute(block, axis, [((i + distance) % size, i) for i in range(size)])


def ring_gather(block, axis, split_axis):
    ahead = shifted(block, axis, 1)
    behind = shifted(block, axis, -1)
    half = block.shape[split_axis] // 2
    far_a = shifted(lax.slice_in_dim(ahead, 0, half, axis=split_axis), axis, 1)
    far_b = shifted(lax.slice_in_dim(behind, half, 2 * half, axis=split_axis), axis, -1)
    far = jnp.concatenate([far_a, far_b], axis=split_axis)
    return [block, ahead, far, behind]


def ordered_by_position(slots, axis, stack_axis):
    size = len(slots)

    def arrangement(at):
        return lambda *blocks: jnp.stack(
            [blocks[(k - at) % size] for k in range(size)], axis=stack_axis
        )

    return lax.switch(lax.axis_index(axis), [arrangement(at) for at in range(size)], *slots)


def per_device(strain, mad_index, mad_table, freq_bins, valid_count):
    channels, win_local, length = strain.shape
    bin_count = freq_bins.shape[0]
    limits = (clip_scales(mad_index, mad_table) * CLIP_FACTOR)[:, None, None]
    bound = limits.astype(strain.dtype)
    clipped = jnp.minimum(jnp.maximum(strain, -bound), bound)
    table = dft_table(freq_bins, length)
    flat_rows = clipped.reshape(channels * win_local, length)
    spectrum = lax.dot_general(
        table, flat_rows, (((0,), (1,)), ((), ())), preferred_element_type=jnp.float32
    )
    freq_index = lax.axis_index("yhi") * lax.axis_size("core") + lax.axis_index("core")
    window_ids = freq_index * win_local + jnp.arange(win_local, dtype=jnp.int32)
    counts = valid_count.astype(jnp.float32)
    weights = jnp.where(
        window_ids[None, :] < valid_count[:, None], 1.0 / jnp.sqrt(counts)[:, None], 0.0
    )
    weighted = (spectrum * weights.reshape(1, channels * win_local)).astype(jnp.bfloat16)
    groups = lax.axis_size("yhi") * lax.axis_size("core")
    pairs = lax.axis_size("ylo")
    bins_local = bin_count // groups
    weighted = weighted.reshape(groups, bins_local * 2, channels * win_local)
    outgoing = jnp.broadcast_to(weighted[None], (pairs,) + weighted.shape)
    outgoing = outgoing.reshape((pairs * groups,) + weighted.shape[1:])
    incoming = lax.all_to_all(outgoing, ("ylo", "yhi", "core"), 0, 0, tiled=True)
    incoming = incoming.reshape(pairs, groups, bins_local, 2, channels, win_local)
    panel = jnp.transpose(incoming, (2, 3, 0, 4, 1, 5)).reshape(
        bins_local, 2, pairs * channels, groups * win_local
    )

    split = (bins_local * 9) // 16
    zs, xs = lax.axis_size("z"), lax.axis_size("x")
    low, high = panel[:split], panel[split:]
    first = ordered_by_position(ring_gather(low, "x", 3), "x", 0)
    second = ordered_by_position(ring_gather(high, "z", 3), "z", 0)
    at = lax.axis_index("ylo") * channels
    rows_low = row_operand(lax.dynamic_slice_in_dim(low, at, channels, axis=2))
    rows_high = row_operand(lax.dynamic_slice_in_dim(high, at, channels, axis=2))
    first, second, rows_low, rows_high = lax.optimization_barrier(
        (first, second, rows_low, rows_high)
    )
    shape = (xs, -1, 2, pairs, channels, groups * win_local)
    width = pairs * channels * xs

    def products(part, block, order):
        block = jnp.transpose(block.reshape(shape), order).reshape(-1, 2, width, groups * win_local)
        return jnp.einsum("fqipw,fpjw->fqij", part, block, preferred_element_type=jnp.float32)

    by_z = [products(rows_low, p, (1, 2, 3, 0, 4, 5)) for p in ring_gather(first, "z", 4)]
    second = [jnp.transpose(p.reshape(shape), (1, 2, 0, 3, 4, 5)) for p in ring_gather(second, "x", 4)]
    second = ordered_by_position(second, "x", 4).reshape(-1, 2, width * zs, groups * win_local)
    high = jnp.einsum(
        "fqipw,fpjw->fqij", rows_high, second, preferred_element_type=jnp.float32
    )

    far = zs // 2
    near = by_z[:far] + [jnp.zeros_like(by_z[far])] + by_z[far + 1:]

    def arrangement(at):
        def build(high, *blocks):
            low = jnp.concatenate([blocks[(k - at) % zs] for k in range(zs)], axis=3)
            return jnp.concatenate([low, high], axis=0)

        return build

    branches = [arrangement(at) for at in range(zs)]
    result = lax.switch(lax.axis_index("z"), branches, high, *near)
    column = ((lax.axis_index("z") + far) % zs) * width
    return lax.dynamic_update_slice(result, by_z[far], (0, 0, 0, column))


def solution(mesh):
    sizes = dict(zip(mesh.axis_names, mesh.devices.shape))
    chan, freq = sizes["chan"], sizes["freq"]
    devices = mesh.devices.reshape(chan // 8, 2, 4, freq // 2, 2)
    grid = Mesh(devices, ("z", "ylo", "x", "yhi", "core"))
    chan_axes = ("z", "ylo", "x")
    freq_axes = ("yhi", "core")
    return jax.shard_map(
        per_device,
        mesh=grid,
        in_specs=(P(chan_axes, freq_axes, None), P(chan_axes), P(), P(), P(chan_axes)),
        out_specs=P(freq_axes, None, chan_axes, None),
        check_vma=False,
    )
```

```python
import math

import jax
import jax.numpy as jnp
from jax import lax
from jax.sharding import Mesh, PartitionSpec as P

CLIP_FACTOR = 2.0


def dft_table(freq_bins, length):
    samples = jnp.arange(length, dtype=jnp.int32)
    phase_index = samples[:, None] * freq_bins[None, :] % length
    angle = phase_index.astype(jnp.float32) * (2.0 * math.pi / length)
    taper = 0.5 - 0.5 * jnp.cos(samples.astype(jnp.float32) * (2.0 * math.pi / length))
    cosine = taper[:, None] * jnp.cos(angle)
    sine = -taper[:, None] * jnp.sin(angle)
    stacked = jnp.stack([cosine, sine], axis=2)
    return stacked.reshape(length, 2 * freq_bins.shape[0]).astype(jnp.bfloat16)


def clip_scales(mad_index, mad_table):
    entries = jnp.arange(mad_table.shape[0], dtype=jnp.int32)
    matches = mad_index[:, None] == entries[None, :]
    return jnp.sum(jnp.where(matches, mad_table[None, :], 0.0), axis=1)


def row_operand(panel):
    first, second = panel[:, 0], panel[:, 1]
    real_rows = jnp.stack([first, second], axis=2)
    imag_rows = jnp.stack([second, -first], axis=2)
    return jnp.stack([real_rows, imag_rows], axis=1)


def shifted(block, axis, distance):
    size = lax.axis_size(axis)
    return lax.ppermute(block, axis, [((i + distance) % size, i) for i in range(size)])


def ring_gather(block, axis, split_axis):
    ahead = shifted(block, axis, 1)
    behind = shifted(block, axis, -1)
    half = block.shape[split_axis] // 2
    far_a = shifted(lax.slice_in_dim(ahead, 0, half, axis=split_axis), axis, 1)
    far_b = shifted(lax.slice_in_dim(behind, half, 2 * half, axis=split_axis), axis, -1)
    far = jnp.concatenate([far_a, far_b], axis=split_axis)
    return [block, ahead, far, behind]


def ordered_by_position(slots, axis, stack_axis):
    size = len(slots)

    def arrangement(at):
        return lambda *blocks: jnp.stack(
            [blocks[(k - at) % size] for k in range(size)], axis=stack_axis
        )

    return lax.switch(lax.axis_index(axis), [arrangement(at) for at in range(size)], *slots)


def per_device(strain, mad_index, mad_table, freq_bins, valid_count):
    channels, win_local, length = strain.shape
    bin_count = freq_bins.shape[0]
    limits = (clip_scales(mad_index, mad_table) * CLIP_FACTOR)[:, None, None]
    bound = limits.astype(strain.dtype)
    clipped = jnp.minimum(jnp.maximum(strain, -bound), bound)
    table = dft_table(freq_bins, length)
    flat_rows = clipped.reshape(channels * win_local, length)
    spectrum = lax.dot_general(
        table, flat_rows, (((0,), (1,)), ((), ())), preferred_element_type=jnp.float32
    )
    freq_index = lax.axis_index("yhi") * lax.axis_size("core") + lax.axis_index("core")
    window_ids = freq_index * win_local + jnp.arange(win_local, dtype=jnp.int32)
    counts = valid_count.astype(jnp.float32)
    weights = jnp.where(
        window_ids[None, :] < valid_count[:, None], 1.0 / jnp.sqrt(counts)[:, None], 0.0
    )
    weighted = (spectrum * weights.reshape(1, channels * win_local)).astype(jnp.bfloat16)
    groups = lax.axis_size("yhi") * lax.axis_size("core")
    pairs = lax.axis_size("ylo")
    bins_local = bin_count // groups
    weighted = weighted.reshape(groups, bins_local * 2, channels * win_local)
    outgoing = jnp.broadcast_to(weighted[None], (pairs,) + weighted.shape)
    outgoing = outgoing.reshape((pairs * groups,) + weighted.shape[1:])
    incoming = lax.all_to_all(outgoing, ("ylo", "yhi", "core"), 0, 0, tiled=True)
    incoming = incoming.reshape(pairs, groups, bins_local, 2, channels, win_local)
    panel = jnp.transpose(incoming, (2, 3, 0, 4, 1, 5)).reshape(
        bins_local, 2, pairs * channels, groups * win_local
    )

    split = (bins_local * 9) // 16
    zs, xs = lax.axis_size("z"), lax.axis_size("x")
    low, high = panel[:split], panel[split:]
    first = ordered_by_position(ring_gather(low, "x", 1), "x", 0)
    second = ordered_by_position(ring_gather(high, "z", 1), "z", 0)
    at = lax.axis_index("ylo") * channels
    rows_low = row_operand(lax.dynamic_slice_in_dim(low, at, channels, axis=2))
    rows_high = row_operand(lax.dynamic_slice_in_dim(high, at, channels, axis=2))
    first, second, rows_low, rows_high = lax.optimization_barrier(
        (first, second, rows_low, rows_high)
    )
    shape = (xs, -1, 2, pairs, channels, groups * win_local)
    width = pairs * channels * xs

    def products(part, block, order):
        block = jnp.transpose(block.reshape(shape), order).reshape(-1, 2, width, groups * win_local)
        return jnp.einsum("fqipw,fpjw->fqij", part, block, preferred_element_type=jnp.float32)

    by_z = [products(rows_low, p, (1, 2, 3, 0, 4, 5)) for p in ring_gather(first, "z", 0)]
    second = [jnp.transpose(p.reshape(shape), (1, 2, 0, 3, 4, 5)) for p in ring_gather(second, "x", 0)]
    second = ordered_by_position(second, "x", 4).reshape(-1, 2, width * zs, groups * win_local)
    high = jnp.einsum(
        "fqipw,fpjw->fqij", rows_high, second, preferred_element_type=jnp.float32
    )

    def arrangement(at):
        def build(high, *blocks):
            low = jnp.concatenate([blocks[(k - at) % zs] for k in range(zs)], axis=3)
            return jnp.concatenate([low, high], axis=0)

        return build

    branches = [arrangement(at) for at in range(zs)]
    return lax.switch(lax.axis_index("z"), branches, high, *by_z)


def solution(mesh):
    sizes = dict(zip(mesh.axis_names, mesh.devices.shape))
    chan, freq = sizes["chan"], sizes["freq"]
    devices = mesh.devices.reshape(chan // 8, 2, 4, freq // 2, 2)
    grid = Mesh(devices, ("z", "ylo", "x", "yhi", "core"))
    chan_axes = ("z", "ylo", "x")
    freq_axes = ("yhi", "core")
    return jax.shard_map(
        per_device,
        mesh=grid,
        in_specs=(P(chan_axes, freq_axes, None), P(chan_axes), P(), P(), P(chan_axes)),
        out_specs=P(freq_axes, None, chan_axes, None),
        check_vma=False,
    )
```

```python
import math

import jax
import jax.numpy as jnp
from jax import lax
from jax.sharding import Mesh, PartitionSpec as P

CLIP_FACTOR = 2.0


def dft_table(freq_bins, length):
    samples = jnp.arange(length, dtype=jnp.int32)
    phase_index = samples[:, None] * freq_bins[None, :] % length
    angle = phase_index.astype(jnp.float32) * (2.0 * math.pi / length)
    taper = 0.5 - 0.5 * jnp.cos(samples.astype(jnp.float32) * (2.0 * math.pi / length))
    cosine = taper[:, None] * jnp.cos(angle)
    sine = -taper[:, None] * jnp.sin(angle)
    stacked = jnp.stack([cosine, sine], axis=2)
    return stacked.reshape(length, 2 * freq_bins.shape[0]).astype(jnp.bfloat16)


def clip_scales(mad_index, mad_table):
    entries = jnp.arange(mad_table.shape[0], dtype=jnp.int32)
    matches = mad_index[:, None] == entries[None, :]
    return jnp.sum(jnp.where(matches, mad_table[None, :], 0.0), axis=1)


def row_operand(panel):
    first, second = panel[:, 0], panel[:, 1]
    real_rows = jnp.stack([first, second], axis=2)
    imag_rows = jnp.stack([second, -first], axis=2)
    return jnp.stack([real_rows, imag_rows], axis=1)


def shifted(block, axis, distance):
    size = lax.axis_size(axis)
    return lax.ppermute(block, axis, [((i + distance) % size, i) for i in range(size)])


def ring_gather(block, axis, split_axis):
    ahead = shifted(block, axis, 1)
    behind = shifted(block, axis, -1)
    half = block.shape[split_axis] // 2
    far_a = shifted(lax.slice_in_dim(ahead, 0, half, axis=split_axis), axis, 1)
    far_b = shifted(lax.slice_in_dim(behind, half, 2 * half, axis=split_axis), axis, -1)
    far = jnp.concatenate([far_a, far_b], axis=split_axis)
    return [block, ahead, far, behind]


def ordered_by_position(slots, axis, stack_axis):
    size = len(slots)

    def arrangement(at):
        return lambda *blocks: jnp.stack(
            [blocks[(k - at) % size] for k in range(size)], axis=stack_axis
        )

    return lax.switch(lax.axis_index(axis), [arrangement(at) for at in range(size)], *slots)


def per_device(strain, mad_index, mad_table, freq_bins, valid_count):
    channels, win_local, length = strain.shape
    bin_count = freq_bins.shape[0]
    limits = (clip_scales(mad_index, mad_table) * CLIP_FACTOR)[:, None, None]
    bound = limits.astype(strain.dtype)
    clipped = jnp.minimum(jnp.maximum(strain, -bound), bound)
    table = dft_table(freq_bins, length)
    flat_rows = clipped.reshape(channels * win_local, length)
    spectrum = lax.dot_general(
        table, flat_rows, (((0,), (1,)), ((), ())), preferred_element_type=jnp.float32
    )
    freq_index = lax.axis_index("yhi") * lax.axis_size("core") + lax.axis_index("core")
    window_ids = freq_index * win_local + jnp.arange(win_local, dtype=jnp.int32)
    counts = valid_count.astype(jnp.float32)
    weights = jnp.where(
        window_ids[None, :] < valid_count[:, None], 1.0 / jnp.sqrt(counts)[:, None], 0.0
    )
    weighted = (spectrum * weights.reshape(1, channels * win_local)).astype(jnp.bfloat16)
    groups = lax.axis_size("yhi") * lax.axis_size("core")
    pairs = lax.axis_size("ylo")
    bins_local = bin_count // groups
    weighted = weighted.reshape(groups, bins_local * 2, channels * win_local)
    outgoing = jnp.broadcast_to(weighted[None], (pairs,) + weighted.shape)
    outgoing = outgoing.reshape((pairs * groups,) + weighted.shape[1:])
    incoming = lax.all_to_all(outgoing, ("ylo", "yhi", "core"), 0, 0, tiled=True)
    incoming = incoming.reshape(pairs, groups, bins_local, 2, channels, win_local)
    panel = jnp.transpose(incoming, (2, 3, 0, 4, 1, 5)).reshape(
        bins_local, 2, pairs * channels, groups * win_local
    )

    split = (bins_local * 9) // 16
    zs, xs = lax.axis_size("z"), lax.axis_size("x")
    low, high = panel[:split], panel[split:]
    first = ordered_by_position(ring_gather(low, "x", 1), "x", 0)
    second = ordered_by_position(ring_gather(high, "z", 1), "z", 0)
    at = lax.axis_index("ylo") * channels
    rows_low = row_operand(lax.dynamic_slice_in_dim(low, at, channels, axis=2))
    rows_high = row_operand(lax.dynamic_slice_in_dim(high, at, channels, axis=2))
    first, rows_low = lax.optimization_barrier((first, rows_low))
    second, rows_high = lax.optimization_barrier((second, rows_high))
    shape = (xs, -1, 2, pairs, channels, groups * win_local)
    width = pairs * channels * xs

    def products(part, block, order):
        block = jnp.transpose(block.reshape(shape), order).reshape(-1, 2, width, groups * win_local)
        return jnp.einsum("fqipw,fpjw->fqij", part, block, preferred_element_type=jnp.float32)

    by_z = [products(rows_low, p, (1, 2, 3, 0, 4, 5)) for p in ring_gather(first, "z", 0)]
    second = [jnp.transpose(p.reshape(shape), (1, 2, 0, 3, 4, 5)) for p in ring_gather(second, "x", 0)]
    second = ordered_by_position(second, "x", 4).reshape(-1, 2, width * zs, groups * win_local)
    high = jnp.einsum(
        "fqipw,fpjw->fqij", rows_high, second, preferred_element_type=jnp.float32
    )

    def arrangement(at):
        def build(high, *blocks):
            low = jnp.concatenate([blocks[(k - at) % zs] for k in range(zs)], axis=3)
            return jnp.concatenate([low, high], axis=0)

        return build

    branches = [arrangement(at) for at in range(zs)]
    return lax.switch(lax.axis_index("z"), branches, high, *by_z)


def solution(mesh):
    sizes = dict(zip(mesh.axis_names, mesh.devices.shape))
    chan, freq = sizes["chan"], sizes["freq"]
    devices = mesh.devices.reshape(chan // 8, 2, 4, freq // 2, 2)
    grid = Mesh(devices, ("z", "ylo", "x", "yhi", "core"))
    chan_axes = ("z", "ylo", "x")
    freq_axes = ("yhi", "core")
    return jax.shard_map(
        per_device,
        mesh=grid,
        in_specs=(P(chan_axes, freq_axes, None), P(chan_axes), P(), P(), P(chan_axes)),
        out_specs=P(freq_axes, None, chan_axes, None),
        check_vma=False,
    )
```

```python
import math

import jax
import jax.numpy as jnp
from jax import lax
from jax.sharding import Mesh, PartitionSpec as P

CLIP_FACTOR = 2.0


def dft_table(freq_bins, length):
    samples = jnp.arange(length, dtype=jnp.int32)
    phase_index = samples[:, None] * freq_bins[None, :] % length
    angle = phase_index.astype(jnp.float32) * (2.0 * math.pi / length)
    taper = 0.5 - 0.5 * jnp.cos(samples.astype(jnp.float32) * (2.0 * math.pi / length))
    cosine = taper[:, None] * jnp.cos(angle)
    sine = -taper[:, None] * jnp.sin(angle)
    stacked = jnp.stack([cosine, sine], axis=2)
    return stacked.reshape(length, 2 * freq_bins.shape[0]).astype(jnp.bfloat16)


def clip_scales(mad_index, mad_table):
    entries = jnp.arange(mad_table.shape[0], dtype=jnp.int32)
    matches = mad_index[:, None] == entries[None, :]
    return jnp.sum(jnp.where(matches, mad_table[None, :], 0.0), axis=1)


def row_operand(panel):
    first, second = panel[:, 0], panel[:, 1]
    real_rows = jnp.stack([first, second], axis=2)
    imag_rows = jnp.stack([second, -first], axis=2)
    return jnp.stack([real_rows, imag_rows], axis=1)


def shifted(block, axis, distance):
    size = lax.axis_size(axis)
    return lax.ppermute(block, axis, [((i + distance) % size, i) for i in range(size)])


def ring_gather(block, axis, split_axis):
    ahead = shifted(block, axis, 1)
    behind = shifted(block, axis, -1)
    half = block.shape[split_axis] // 2
    far_a = shifted(lax.slice_in_dim(ahead, 0, half, axis=split_axis), axis, 1)
    far_b = shifted(lax.slice_in_dim(behind, half, 2 * half, axis=split_axis), axis, -1)
    far = jnp.concatenate([far_a, far_b], axis=split_axis)
    return [block, ahead, far, behind]


def ordered_by_position(slots, axis, stack_axis):
    size = len(slots)

    def arrangement(at):
        return lambda *blocks: jnp.stack(
            [blocks[(k - at) % size] for k in range(size)], axis=stack_axis
        )

    return lax.switch(lax.axis_index(axis), [arrangement(at) for at in range(size)], *slots)


def per_device(strain, mad_index, mad_table, freq_bins, valid_count):
    channels, win_local, length = strain.shape
    bin_count = freq_bins.shape[0]
    limits = (clip_scales(mad_index, mad_table) * CLIP_FACTOR)[:, None, None]
    bound = limits.astype(strain.dtype)
    clipped = jnp.minimum(jnp.maximum(strain, -bound), bound)
    table = dft_table(freq_bins, length)
    flat_rows = clipped.reshape(channels * win_local, length)
    spectrum = lax.dot_general(
        table, flat_rows, (((0,), (1,)), ((), ())), preferred_element_type=jnp.float32
    )
    freq_index = lax.axis_index("yhi") * lax.axis_size("core") + lax.axis_index("core")
    window_ids = freq_index * win_local + jnp.arange(win_local, dtype=jnp.int32)
    counts = valid_count.astype(jnp.float32)
    weights = jnp.where(
        window_ids[None, :] < valid_count[:, None], 1.0 / jnp.sqrt(counts)[:, None], 0.0
    )
    weighted = (spectrum * weights.reshape(1, channels * win_local)).astype(jnp.bfloat16)
    groups = lax.axis_size("yhi") * lax.axis_size("core")
    pairs = lax.axis_size("ylo")
    bins_local = bin_count // groups
    weighted = weighted.reshape(groups, bins_local * 2, channels * win_local)
    outgoing = jnp.broadcast_to(weighted[None], (pairs,) + weighted.shape)
    outgoing = outgoing.reshape((pairs * groups,) + weighted.shape[1:])
    incoming = lax.all_to_all(outgoing, ("ylo", "yhi", "core"), 0, 0, tiled=True)
    incoming = incoming.reshape(pairs, groups, bins_local, 2, channels, win_local)
    panel = jnp.transpose(incoming, (2, 3, 0, 4, 1, 5)).reshape(
        bins_local, 2, pairs * channels, groups * win_local
    )

    split = (bins_local * 9) // 16
    zs, xs = lax.axis_size("z"), lax.axis_size("x")
    low, high = panel[:split], panel[split:]
    first = ordered_by_position(ring_gather(low, "x", 1), "x", 0)
    second = ordered_by_position(ring_gather(high, "z", 1), "z", 0)
    at = lax.axis_index("ylo") * channels
    rows_low = row_operand(lax.dynamic_slice_in_dim(low, at, channels, axis=2))
    rows_high = row_operand(lax.dynamic_slice_in_dim(high, at, channels, axis=2))
    first, rows_low = lax.optimization_barrier((first, rows_low))
    second, rows_high = lax.optimization_barrier((second, rows_high))
    shape = (xs, -1, 2, pairs, channels, groups * win_local)
    width = pairs * channels * xs

    def products(part, block, order):
        block = jnp.transpose(block.reshape(shape), order).reshape(-1, 2, width, groups * win_local)
        return jnp.einsum("fqipw,fpjw->fqij", part, block, preferred_element_type=jnp.float32)

    by_z = [products(rows_low, p, (1, 2, 3, 0, 4, 5)) for p in ring_gather(first, "z", 0)]
    second = [jnp.transpose(p.reshape(shape), (1, 2, 0, 3, 4, 5)) for p in ring_gather(second, "x", 0)]
    second = [p.reshape(p.shape[0], 2, zs * pairs, channels, groups * win_local) for p in second]
    second = ordered_by_position(second, "x", 3).reshape(-1, 2, width * zs, groups * win_local)
    high = jnp.einsum(
        "fqipw,fpjw->fqij", rows_high, second, preferred_element_type=jnp.float32
    )

    def arrangement(at):
        def build(high, *blocks):
            low = jnp.concatenate([blocks[(k - at) % zs] for k in range(zs)], axis=3)
            return jnp.concatenate([low, high], axis=0)

        return build

    branches = [arrangement(at) for at in range(zs)]
    return lax.switch(lax.axis_index("z"), branches, high, *by_z)


def solution(mesh):
    sizes = dict(zip(mesh.axis_names, mesh.devices.shape))
    chan, freq = sizes["chan"], sizes["freq"]
    devices = mesh.devices.reshape(chan // 8, 2, 4, freq // 2, 2)
    grid = Mesh(devices, ("z", "ylo", "x", "yhi", "core"))
    chan_axes = ("z", "ylo", "x")
    freq_axes = ("yhi", "core")
    return jax.shard_map(
        per_device,
        mesh=grid,
        in_specs=(P(chan_axes, freq_axes, None), P(chan_axes), P(), P(), P(chan_axes)),
        out_specs=P(freq_axes, None, chan_axes, None),
        check_vma=False,
    )
```
